512 devices in a mesh: grp: 8 (over z_lo, core), spec: 64 (over z_hi, x, y).
Axes of the slice: x: 4, y: 4, z: 16 (z_hi: 4, z_lo: 4; z = z_hi * 4 + z_lo), core: 2. Of those that a mesh axis runs over, the one named last changes fastest.
Arguments:
- queries: bfloat16 [262144, 1024], P(('grp', 'spec')), may hold values from -6 to 6
- out_grad: bfloat16 [262144, 1024], P(('grp', 'spec')), may hold values from -48 to 48
- spec_keys: bfloat16 [512, 192, 1024], P(('grp', 'spec')), may hold values from -6 to 6
- spec_values: bfloat16 [512, 192, 1024], P(('grp', 'spec')), may hold values from -6 to 6
- owner_of: int32 [32768, 1], P(('grp', 'spec')), may hold values from 0 to 63; in each aligned block of 64 rows (0 to 63, 64 to 127, ...) at most 2 rows name the same one
- query_gain: float32 [1024], replicated, may hold values from 0.5 to 1.5
Outputs:
- query_grad: bfloat16 [262144, 1024], P(('grp', 'spec'))
- key_grad: bfloat16 [512, 192, 1024], P(('grp', 'spec'))
- value_grad: bfloat16 [512, 192, 1024], P(('grp', 'spec'))
- gain_grad: float32 [1024], replicated
The draws below stay inside these ranges and needn't reach their ends.
Inputs may be any that keep to these rules, and one draw needn't show every extreme that they name: `owner_of`: among the candidates of one device, at most 2 name the same spec.
All inputs are finite; a program needn't handle non-finite values.
Results may differ from the reference program's by a relative error of at most 0.012.
The reference program's roundings to bfloat16 on the way (of `gained`, `probs_b` and `dscores`) count: a program that leaves them out, or rounds other values in their place, can miss the bound.
Values may be sent and summed in bfloat16 or wider, within the bound.
No kernel may reach another device: no remote copies, remote signals or barrier semaphores. Data moves between devices by JAX's collectives and lax.ppermute only.
A program may use at most 64 MiB of HBM per device.

```python
import math
import jax
import jax.numpy as jnp
import numpy as np
from jax import lax

HEADS = 8
HEAD_DIM = 128
QTOK = 8
KEYS = 192
CAP = 2
CAND_DEV = 64
CANDS = 32768
ROWS = 262144
SPECS = 512
N_SPEC = 64


def draw_queries(key, part):
    width = HEADS * HEAD_DIM
    total_rows = CANDS * QTOK
    first = jax.random.fold_in(key, 1)
    base = jnp.clip(jax.random.normal(first, (total_rows, width), jnp.float32), -6.0, 6.0)
    return base.astype(jnp.bfloat16)


def draw_spec_keys(key, part):
    width = HEADS * HEAD_DIM
    first = jax.random.fold_in(key, 3)
    base = jnp.clip(jax.random.normal(first, (SPECS, KEYS, width), jnp.float32), -6.0, 6.0)
    return base.astype(jnp.bfloat16)


def level_of(own_key, dims, shards, least, high):
    def one(dim, shards_of):
        steps = jax.random.uniform(jax.random.fold_in(jax.random.fold_in(own_key, 6), dim), (shards_of,), jnp.float32, least / len(shards), high / len(shards))
        return jnp.repeat(jnp.exp(steps), dims[dim] // shards_of).reshape((-1,) + (1,) * (len(dims) - dim - 1))

    gain = one(*shards[0])
    for cut in shards[1:]:
        gain = gain * one(*cut)
    return gain


def assign_block(key, own, number, rows, count, top, most, skew):
    sequence = jax.random.permutation(key, count)
    packed, ordinary = load_shares(count, rows * top, most, skew, True), load_shares(count, rows * top, most, skew, False)
    places = jnp.arange(count)

    def named(lengths, rotation):
        used = int((lengths > 0).sum())
        fixed = max(1, used // 4)
        shifted = fixed + (places - fixed + rotation * (used - fixed)) % max(1, count - fixed)
        return jnp.zeros((count,), jnp.int32).at[sequence[jnp.where(places < fixed, places, shifted)]].set(jnp.asarray(lengths, jnp.int32))

    lengths = jnp.where(number % 4 == 0, named(packed, number // 4), named(ordinary, number - number // 4 - 1))
    mixed = jax.random.permutation(jax.random.fold_in(own, 3), count)
    giver, taker = mixed[0:count // 2 * 2:2], mixed[1:count // 2 * 2:2]
    room = jnp.minimum(lengths[giver] - 1, most - lengths[taker]) // 2
    room = jnp.where((giver == sequence[0]) | (taker == sequence[0]) | (lengths[taker] == 0), 0, jnp.maximum(room, 0))
    shifted = jax.random.randint(jax.random.fold_in(own, 4), (count // 2,), 0, 1 << 20) % (room + 1)
    lengths = lengths.at[giver].add(-shifted).at[taker].add(shifted)
    items = jnp.searchsorted(jnp.cumsum(lengths), jnp.arange(rows * top), side="right").astype(jnp.int32)
    table = items.reshape(top, rows).T
    table = table[jax.random.permutation(jax.random.fold_in(own, 1), rows)]
    rotation = jax.random.randint(jax.random.fold_in(own, 2), (rows, 1), 0, top)
    return jnp.take_along_axis(table, (jnp.arange(top)[None, :] + rotation) % top, axis=1)


def load_shares(count, total, most, skew, full):
    loads = [(1 << 20) // math.isqrt(standing ** skew) + 1 for standing in range(1, count + 1)]
    largest = most if full else min(most, max(-(-total // count), total * loads[0] // sum(loads)))
    least = 1 if total - largest >= count - 1 else 0
    holding, spare = [largest] + [least] * (count - 1), total - largest - least * (count - 1)
    while spare > 0:
        free = [i for i in range(1, count) if holding[i] < largest] or [i for i in range(1, count) if holding[i] < most]
        mass, left = sum([loads[i] for i in free]), spare
        for i in free:
            addition = min(most - holding[i], max(1, left * loads[i] // mass), spare)
            holding[i] = holding[i] + addition
            spare = spare - addition
    return np.array(holding)


def centred(stream_key, shape, scale, reach, cuts=(), kind=jnp.bfloat16):
    array = scale * jax.random.normal(stream_key, shape, jnp.float32)
    if cuts:
        array = array * level_of(stream_key, shape, cuts, -0.22, 0.18)
    return jnp.clip(array, -reach, reach).astype(kind)


def setup_inputs(seed: int = 0) -> dict:
    streams_of = jax.random.split(jax.random.key(seed), 7)
    queries = draw_queries(jax.random.fold_in(streams_of[6], 71), 0)
    out_grad = centred(streams_of[1], (ROWS, HEADS * HEAD_DIM), 8.0, 48.0, ((0, 512),))
    spec_keys = draw_spec_keys(jax.random.fold_in(streams_of[6], 71), 0)
    spec_values = centred(streams_of[3], (SPECS, KEYS, HEADS * HEAD_DIM), 1.0, 6.0, ((0, 512),))
    owner_of_keys = jax.random.split(jax.random.fold_in(streams_of[4], 1), CANDS // CAND_DEV)
    owner_of_turns = jax.random.permutation(jax.random.fold_in(streams_of[4], 3), CANDS // CAND_DEV)
    owner_of = jax.vmap(lambda own, number: assign_block(jax.random.fold_in(streams_of[4], 2), own, number, CAND_DEV, N_SPEC, 1, CAP, 2))(owner_of_keys, owner_of_turns).reshape((CANDS, 1))
    query_gain = jnp.clip(1.0 + 0.1 * jax.random.normal(streams_of[5], (HEADS * HEAD_DIM,), jnp.float32), 0.5, 1.5)
    return {"queries": queries, "out_grad": out_grad, "spec_keys": spec_keys, "spec_values": spec_values, "owner_of": owner_of, "query_gain": query_gain}


def reference(queries, out_grad, spec_keys, spec_values, owner_of, query_gain):
    width = HEADS * HEAD_DIM
    inv_root = 1.0 / math.sqrt(HEAD_DIM)
    per_group = CAND_DEV * N_SPEC
    cand_ids = jnp.arange(CANDS, dtype=jnp.int32)
    spec_ids = (cand_ids // per_group * N_SPEC + owner_of[:, 0]).astype(jnp.int32)
    gained = (queries.astype(jnp.float32) * query_gain).astype(jnp.bfloat16)
    gained = gained.reshape(CANDS, QTOK, HEADS, HEAD_DIM)
    raw_rows = queries.reshape(CANDS, QTOK, HEADS, HEAD_DIM)
    grad_rows = out_grad.reshape(CANDS, QTOK, HEADS, HEAD_DIM)
    turns = CANDS // CAND_DEV

    def advance(carry, index):
        key_acc, value_acc, gain_acc = carry
        start = (index * CAND_DEV).astype(jnp.int32)
        ids = lax.dynamic_slice_in_dim(spec_ids, start, CAND_DEV, 0).astype(jnp.int32)
        q_block = lax.dynamic_slice_in_dim(gained, start, CAND_DEV, 0).astype(jnp.float32)
        raw_block = lax.dynamic_slice_in_dim(raw_rows, start, CAND_DEV, 0).astype(jnp.float32)
        g_block = lax.dynamic_slice_in_dim(grad_rows, start, CAND_DEV, 0).astype(jnp.float32)
        k_block = spec_keys[ids].reshape(CAND_DEV, KEYS, HEADS, HEAD_DIM).astype(jnp.float32)
        v_block = spec_values[ids].reshape(CAND_DEV, KEYS, HEADS, HEAD_DIM).astype(jnp.float32)
        scores = jnp.einsum('bqhd,blhd->bhql', q_block, k_block) * inv_root
        top = lax.optimization_barrier(jnp.max(scores, axis=-1, keepdims=True))
        expo = jnp.exp(scores - top)
        probs = expo / lax.optimization_barrier(jnp.sum(expo, axis=-1, keepdims=True))
        probs_b = probs.astype(jnp.bfloat16).astype(jnp.float32)
        attended = jnp.einsum('bhql,blhd->bqhd', probs_b, v_block)
        delta = lax.optimization_barrier(jnp.sum(g_block * attended, axis=-1))
        dprobs = jnp.einsum('bqhd,blhd->bhql', g_block, v_block)
        dscores = (probs * (dprobs - jnp.transpose(delta, (0, 2, 1))[..., None])).astype(jnp.bfloat16).astype(jnp.float32)
        gained_grad = jnp.einsum('bhql,blhd->bqhd', dscores, k_block) * inv_root
        key_part = jnp.einsum('bhql,bqhd->blhd', dscores, q_block) * inv_root
        value_part = jnp.einsum('bhql,bqhd->blhd', probs_b, g_block)
        key_acc = key_acc.at[ids].add(key_part.reshape(CAND_DEV, KEYS, width))
        value_acc = value_acc.at[ids].add(value_part.reshape(CAND_DEV, KEYS, width))
        gained_flat = gained_grad.reshape(CAND_DEV * QTOK, width)
        gain_acc = gain_acc + lax.optimization_barrier(jnp.sum(raw_block.reshape(CAND_DEV * QTOK, width) * gained_flat, axis=0))
        q_out = (gained_flat * query_gain).astype(jnp.bfloat16)
        return ((key_acc, value_acc, gain_acc), q_out)
    start_carry = (jnp.zeros((SPECS, KEYS, width), jnp.float32), jnp.zeros((SPECS, KEYS, width), jnp.float32), jnp.zeros((width,), jnp.float32))
    final, q_blocks = lax.scan(advance, start_carry, jnp.arange(turns, dtype=jnp.int32))
    key_acc, value_acc, gain_acc = final
    query_grad = q_blocks.reshape(ROWS, width)
    return (query_grad, key_acc.astype(jnp.bfloat16), value_acc.astype(jnp.bfloat16), gain_acc)
```

```python
import math

import jax
import jax.numpy as jnp
from jax import lax
from jax.sharding import PartitionSpec as P

HEADS = 8
HEAD_DIM = 128
CAP = 2


def attend_backward(recv_rows, recv_grads, keys_here, values_here, query_gain):
    total_rows, width = recv_rows.shape
    head_dim = width // HEADS
    inv_root = 1.0 / math.sqrt(HEAD_DIM)
    gained = (recv_rows.astype(jnp.float32) * query_gain).astype(jnp.bfloat16)
    key_count = keys_here.shape[0]
    q_heads = gained.reshape(total_rows, HEADS, head_dim)
    g_heads = recv_grads.reshape(total_rows, HEADS, head_dim)
    k_heads = keys_here.reshape(key_count, HEADS, head_dim)
    v_heads = values_here.reshape(key_count, HEADS, head_dim)
    f32 = jnp.float32
    scores = jnp.einsum("rhd,khd->hrk", q_heads, k_heads, preferred_element_type=f32) * inv_root
    top = jnp.max(scores, axis=2, keepdims=True)
    expo = jnp.exp(scores - top)
    probs = expo / jnp.sum(expo, axis=2, keepdims=True)
    probs_b = probs.astype(jnp.bfloat16)
    attended = jnp.einsum("hrk,khd->rhd", probs_b, v_heads, preferred_element_type=f32)
    delta = jnp.sum(g_heads.astype(f32) * attended, axis=2)
    dprobs = jnp.einsum("rhd,khd->hrk", g_heads, v_heads, preferred_element_type=f32)
    dscores = (probs * (dprobs - delta.T[:, :, None])).astype(jnp.bfloat16)
    q_grad = jnp.einsum("hrk,khd->rhd", dscores, k_heads, preferred_element_type=f32) * inv_root
    k_grad = jnp.einsum("hrk,rhd->khd", dscores, q_heads, preferred_element_type=f32) * inv_root
    v_grad = jnp.einsum("hrk,rhd->khd", probs_b, g_heads, preferred_element_type=f32)
    gained_grad = q_grad.reshape(total_rows, width)
    return (gained_grad, k_grad.reshape(key_count, width), v_grad.reshape(key_count, width))


def shards(queries, out_grad, spec_keys, spec_values, owner_of, query_gain):
    peers = lax.axis_size("spec")
    cand_count = owner_of.shape[0]
    width = queries.shape[1]
    qtok_here = queries.shape[0] // cand_count
    target = owner_of[:, 0]
    onehot = (target[:, None] == jnp.arange(peers, dtype=jnp.int32)[None, :]).astype(jnp.int32)
    earlier = jnp.cumsum(onehot, axis=0) - onehot
    position = jnp.sum(earlier * onehot, axis=1)
    flat_both = jnp.concatenate(
        [queries.reshape(cand_count, qtok_here * width), out_grad.reshape(cand_count, qtok_here * width)],
        axis=1,
    )
    keys_here, values_here = spec_keys[0], spec_values[0]
    home_grads = None
    key_acc = None
    value_acc = None
    gain_acc = None
    for slot in range(CAP):
        placing = (
            (jnp.arange(peers, dtype=jnp.int32)[:, None] == target[None, :])
            & (position[None, :] == slot)
        ).astype(jnp.bfloat16)
        send_both = jnp.dot(placing, flat_both, preferred_element_type=jnp.float32).astype(
            jnp.bfloat16
        )
        recv_both = lax.all_to_all(send_both, "spec", split_axis=0, concat_axis=0, tiled=True)
        recv_rows = recv_both[:, : qtok_here * width].reshape(peers * qtok_here, width)
        recv_cotan = recv_both[:, qtok_here * width :].reshape(peers * qtok_here, width)
        gained_grad, key_part, value_part = attend_backward(
            recv_rows, recv_cotan, keys_here, values_here, query_gain
        )
        gain_part = jnp.sum(recv_rows.astype(jnp.float32) * gained_grad, axis=0)
        going_back = (
            (gained_grad * query_gain).astype(jnp.bfloat16).reshape(peers, qtok_here * width)
        )
        came_back = lax.all_to_all(going_back, "spec", split_axis=0, concat_axis=0, tiled=True)
        home_part = jnp.dot(placing.T, came_back, preferred_element_type=jnp.float32)
        if home_grads is None:
            home_grads, key_acc, value_acc, gain_acc = home_part, key_part, value_part, gain_part
        else:
            home_grads = home_grads + home_part
            key_acc = key_acc + key_part
            value_acc = value_acc + value_part
            gain_acc = gain_acc + gain_part
    gain_grad = lax.psum(gain_acc, ("grp", "spec"))
    query_grad = home_grads.astype(jnp.bfloat16).reshape(cand_count * qtok_here, width)
    key_grad = key_acc.astype(jnp.bfloat16)
    value_grad = value_acc.astype(jnp.bfloat16)
    return (query_grad, key_grad[None], value_grad[None], gain_grad)


def solution(mesh):
    return jax.shard_map(
        shards,
        mesh=mesh,
        in_specs=(
            P(("grp", "spec"), None),
            P(("grp", "spec"), None),
            P(("grp", "spec"), None, None),
            P(("grp", "spec"), None, None),
            P(("grp", "spec"), None),
            P(),
        ),
        out_specs=(
            P(("grp", "spec"), None),
            P(("grp", "spec"), None, None),
            P(("grp", "spec"), None, None),
            P(),
        ),
        check_vma=False,
    )
```

```python
import math

import jax
import jax.numpy as jnp
from jax import lax
from jax.sharding import PartitionSpec as P

HEADS = 8
HEAD_DIM = 128
CAP = 2
PIECES = 3


def attend_backward(recv_rows, recv_grads, keys_here, values_here, query_gain):
    total_rows, width = recv_rows.shape
    head_dim = width // HEADS
    inv_root = 1.0 / math.sqrt(HEAD_DIM)
    gained = (recv_rows.astype(jnp.float32) * query_gain).astype(jnp.bfloat16)
    key_count = keys_here.shape[0]
    q_heads = gained.reshape(total_rows, HEADS, head_dim)
    g_heads = recv_grads.reshape(total_rows, HEADS, head_dim)
    k_heads = keys_here.reshape(key_count, HEADS, head_dim)
    v_heads = values_here.reshape(key_count, HEADS, head_dim)
    f32 = jnp.float32
    scores = jnp.einsum("rhd,khd->hrk", q_heads, k_heads, preferred_element_type=f32) * inv_root
    top = jnp.max(scores, axis=2, keepdims=True)
    expo = jnp.exp(scores - top)
    probs = expo / jnp.sum(expo, axis=2, keepdims=True)
    probs_b = probs.astype(jnp.bfloat16)
    attended = jnp.einsum("hrk,khd->rhd", probs_b, v_heads, preferred_element_type=f32)
    delta = jnp.sum(g_heads.astype(f32) * attended, axis=2)
    dprobs = jnp.einsum("rhd,khd->hrk", g_heads, v_heads, preferred_element_type=f32)
    dscores = (probs * (dprobs - delta.T[:, :, None])).astype(jnp.bfloat16)
    q_grad = jnp.einsum("hrk,khd->rhd", dscores, k_heads, preferred_element_type=f32) * inv_root
    k_grad = jnp.einsum("hrk,rhd->khd", dscores, q_heads, preferred_element_type=f32) * inv_root
    v_grad = jnp.einsum("hrk,rhd->khd", probs_b, g_heads, preferred_element_type=f32)
    gained_grad = q_grad.reshape(total_rows, width)
    return (gained_grad, k_grad.reshape(key_count, width), v_grad.reshape(key_count, width))


def split_pieces(value, count):
    pieces = []
    rest = value
    for _ in range(count - 1):
        head = lax.reduce_precision(rest, exponent_bits=8, mantissa_bits=7)
        pieces.append(head)
        rest = rest - head
    pieces.append(rest)
    return jnp.stack(pieces).astype(jnp.bfloat16)


def shards(queries, out_grad, spec_keys, spec_values, owner_of, query_gain):
    peers = lax.axis_size("spec")
    cand_count = owner_of.shape[0]
    width = queries.shape[1]
    qtok_here = queries.shape[0] // cand_count
    slot_count = peers * CAP
    target = owner_of[:, 0]
    onehot = (target[:, None] == jnp.arange(peers, dtype=jnp.int32)[None, :]).astype(jnp.int32)
    earlier = jnp.cumsum(onehot, axis=0) - onehot
    position = jnp.sum(earlier * onehot, axis=1)
    slot_index = target * CAP + position
    placing = (jnp.arange(slot_count, dtype=jnp.int32)[:, None] == slot_index[None, :]).astype(
        jnp.bfloat16
    )
    flat_both = jnp.concatenate(
        [queries.reshape(cand_count, qtok_here * width), out_grad.reshape(cand_count, qtok_here * width)],
        axis=1,
    )
    send_both = jnp.dot(placing, flat_both, preferred_element_type=jnp.float32).astype(jnp.bfloat16)
    send_both = send_both.reshape(peers, CAP * 2 * qtok_here, width)
    recv_both = lax.all_to_all(send_both, "spec", split_axis=0, concat_axis=0, tiled=True)
    recv_both = recv_both.reshape(slot_count, 2, qtok_here, width)
    recv_rows = recv_both[:, 0].reshape(slot_count * qtok_here, width)
    recv_cotan = recv_both[:, 1].reshape(slot_count * qtok_here, width)
    gained_grad, key_grad, value_grad = attend_backward(
        recv_rows, recv_cotan, spec_keys[0], spec_values[0], query_gain
    )
    partial_value = jnp.sum(recv_rows.astype(jnp.float32) * gained_grad, axis=0)
    going_back = (gained_grad * query_gain).astype(jnp.bfloat16).reshape(
        peers, CAP * qtok_here, width
    )
    gain_rows = jnp.broadcast_to(split_pieces(partial_value, PIECES)[None], (peers, PIECES, width))
    going_back = jnp.concatenate([going_back, gain_rows], axis=1)
    came_back = lax.all_to_all(going_back, "spec", split_axis=0, concat_axis=0, tiled=True)
    spec_sum = jnp.sum(came_back[:, CAP * qtok_here :].astype(jnp.float32), axis=(0, 1))
    gain_grad = lax.psum(spec_sum, "grp")
    came_back = came_back[:, : CAP * qtok_here]
    home_grads = jnp.dot(
        placing.T, came_back.reshape(slot_count, qtok_here * width), preferred_element_type=jnp.float32
    ).astype(jnp.bfloat16)
    query_grad = home_grads.reshape(cand_count * qtok_here, width)
    return (
        query_grad,
        key_grad.astype(jnp.bfloat16)[None],
        value_grad.astype(jnp.bfloat16)[None],
        gain_grad,
    )


def solution(mesh):
    return jax.shard_map(
        shards,
        mesh=mesh,
        in_specs=(
            P(("grp", "spec"), None),
            P(("grp", "spec"), None),
            P(("grp", "spec"), None, None),
            P(("grp", "spec"), None, None),
            P(("grp", "spec"), None),
            P(),
        ),
        out_specs=(
            P(("grp", "spec"), None),
            P(("grp", "spec"), None, None),
            P(("grp", "spec"), None, None),
            P(),
        ),
        check_vma=False,
    )
```

```python
import math

import jax
import jax.numpy as jnp
from jax import lax
from jax.sharding import PartitionSpec as P

HEADS = 8
HEAD_DIM = 128
CAP = 2
PIECES = 2


def attend_backward(recv_rows, recv_grads, keys_here, values_here, query_gain):
    total_rows, width = recv_rows.shape
    head_dim = width // HEADS
    inv_root = 1.0 / math.sqrt(HEAD_DIM)
    gained = (recv_rows.astype(jnp.float32) * query_gain).astype(jnp.bfloat16)
    key_count = keys_here.shape[0]
    q_heads = gained.reshape(total_rows, HEADS, head_dim)
    g_heads = recv_grads.reshape(total_rows, HEADS, head_dim)
    k_heads = keys_here.reshape(key_count, HEADS, head_dim)
    v_heads = values_here.reshape(key_count, HEADS, head_dim)
    f32 = jnp.float32
    scores = jnp.einsum("rhd,khd->hrk", q_heads, k_heads, preferred_element_type=f32) * inv_root
    top = jnp.max(scores, axis=2, keepdims=True)
    expo = jnp.exp(scores - top)
    probs = expo / jnp.sum(expo, axis=2, keepdims=True)
    probs_b = probs.astype(jnp.bfloat16)
    attended = jnp.einsum("hrk,khd->rhd", probs_b, v_heads, preferred_element_type=f32)
    delta = jnp.sum(g_heads.astype(f32) * attended, axis=2)
    dprobs = jnp.einsum("rhd,khd->hrk", g_heads, v_heads, preferred_element_type=f32)
    dscores = (probs * (dprobs - delta.T[:, :, None])).astype(jnp.bfloat16)
    q_grad = jnp.einsum("hrk,khd->rhd", dscores, k_heads, preferred_element_type=f32) * inv_root
    k_grad = jnp.einsum("hrk,rhd->khd", dscores, q_heads, preferred_element_type=f32) * inv_root
    v_grad = jnp.einsum("hrk,rhd->khd", probs_b, g_heads, preferred_element_type=f32)
    gained_grad = q_grad.reshape(total_rows, width)
    return (gained_grad, k_grad.reshape(key_count, width), v_grad.reshape(key_count, width))


def split_pieces(value, count):
    pieces = []
    rest = value
    for _ in range(count - 1):
        head = lax.reduce_precision(rest, exponent_bits=8, mantissa_bits=7)
        pieces.append(head)
        rest = rest - head
    pieces.append(rest)
    return jnp.stack(pieces).astype(jnp.bfloat16)


def shards(queries, out_grad, spec_keys, spec_values, owner_of, query_gain):
    peers = lax.axis_size("spec")
    cand_count = owner_of.shape[0]
    width = queries.shape[1]
    qtok_here = queries.shape[0] // cand_count
    slot_count = peers * CAP
    target = owner_of[:, 0]
    onehot = (target[:, None] == jnp.arange(peers, dtype=jnp.int32)[None, :]).astype(jnp.int32)
    earlier = jnp.cumsum(onehot, axis=0) - onehot
    position = jnp.sum(earlier * onehot, axis=1)
    slot_index = target * CAP + position
    matches = jnp.arange(slot_count, dtype=jnp.int32)[:, None] == slot_index[None, :]
    source = jnp.argmax(matches, axis=1).astype(jnp.int32)
    used = jnp.any(matches, axis=1)
    both = jnp.concatenate(
        [queries.reshape(cand_count, qtok_here, width), out_grad.reshape(cand_count, qtok_here, width)],
        axis=1,
    )
    send_both = jnp.where(used[:, None, None], jnp.take(both, source, axis=0), jnp.zeros((), both.dtype))
    send_both = send_both.reshape(peers, CAP * 2 * qtok_here, width)
    recv_both = lax.all_to_all(send_both, "spec", split_axis=0, concat_axis=0, tiled=True)
    recv_both = recv_both.reshape(slot_count, 2, qtok_here, width)
    recv_rows = recv_both[:, 0].reshape(slot_count * qtok_here, width)
    recv_cotan = recv_both[:, 1].reshape(slot_count * qtok_here, width)
    gained_grad, key_grad, value_grad = attend_backward(
        recv_rows, recv_cotan, spec_keys[0], spec_values[0], query_gain
    )
    partial_value = jnp.sum(recv_rows.astype(jnp.float32) * gained_grad, axis=0)
    going_back = (gained_grad * query_gain).astype(jnp.bfloat16).reshape(
        peers, CAP * qtok_here, width
    )
    gain_rows = jnp.broadcast_to(split_pieces(partial_value, PIECES)[None], (peers, PIECES, width))
    going_back = jnp.concatenate([going_back, gain_rows], axis=1)
    came_back = lax.all_to_all(going_back, "spec", split_axis=0, concat_axis=0, tiled=True)
    spec_sum = jnp.sum(came_back[:, CAP * qtok_here :].astype(jnp.float32), axis=(0, 1))
    gain_grad = lax.psum(spec_sum, "grp")
    came_back = came_back[:, : CAP * qtok_here]
    home_grads = jnp.take(came_back.reshape(slot_count, qtok_here, width), slot_index, axis=0)
    query_grad = home_grads.reshape(cand_count * qtok_here, width)
    return (
        query_grad,
        key_grad.astype(jnp.bfloat16)[None],
        value_grad.astype(jnp.bfloat16)[None],
        gain_grad,
    )


def solution(mesh):
    return jax.shard_map(
        shards,
        mesh=mesh,
        in_specs=(
            P(("grp", "spec"), None),
            P(("grp", "spec"), None),
            P(("grp", "spec"), None, None),
            P(("grp", "spec"), None, None),
            P(("grp", "spec"), None),
            P(),
        ),
        out_specs=(
            P(("grp", "spec"), None),
            P(("grp", "spec"), None, None),
            P(("grp", "spec"), None, None),
            P(),
        ),
        check_vma=False,
    )
```

```python
import math

import jax
import jax.numpy as jnp
from jax import lax
from jax.sharding import PartitionSpec as P

HEADS = 8
HEAD_DIM = 128
CAP = 2
PIECES = 2


def attend_backward(recv_rows, recv_grads, keys_here, values_here, query_gain):
    total_rows, width = recv_rows.shape
    head_dim = width // HEADS
    key_count = keys_here.shape[0]
    inv_root = 1.0 / math.sqrt(HEAD_DIM)
    f32 = jnp.float32
    gain_hm = query_gain.reshape(HEADS, 1, head_dim)
    raw_hm = recv_rows.reshape(total_rows, HEADS, head_dim).transpose(1, 0, 2)
    g_hm = recv_grads.reshape(total_rows, HEADS, head_dim).transpose(1, 0, 2)
    k_hm = keys_here.reshape(key_count, HEADS, head_dim).transpose(1, 0, 2)
    v_hm = values_here.reshape(key_count, HEADS, head_dim).transpose(1, 0, 2)
    gained_hm = (raw_hm.astype(f32) * gain_hm).astype(jnp.bfloat16)
    scores = jnp.einsum("hrd,hkd->hrk", gained_hm, k_hm, preferred_element_type=f32) * inv_root
    top = jnp.max(scores, axis=2, keepdims=True)
    expo = jnp.exp(scores - top)
    probs = expo / jnp.sum(expo, axis=2, keepdims=True)
    probs_b = probs.astype(jnp.bfloat16)
    attended = jnp.einsum("hrk,hkd->hrd", probs_b, v_hm, preferred_element_type=f32)
    delta = jnp.sum(g_hm.astype(f32) * attended, axis=2, keepdims=True)
    dprobs = jnp.einsum("hrd,hkd->hrk", g_hm, v_hm, preferred_element_type=f32)
    dscores = (probs * (dprobs - delta)).astype(jnp.bfloat16)
    q_grad = jnp.einsum("hrk,hkd->hrd", dscores, k_hm, preferred_element_type=f32) * inv_root
    k_grad = jnp.einsum("hrk,hrd->hkd", dscores, gained_hm, preferred_element_type=f32) * inv_root
    v_grad = jnp.einsum("hrk,hrd->hkd", probs_b, g_hm, preferred_element_type=f32)
    gain_part = jnp.sum(raw_hm.astype(f32) * q_grad, axis=1).reshape(width)
    going_back = (q_grad * gain_hm).astype(jnp.bfloat16).transpose(1, 0, 2).reshape(total_rows, width)
    key_grad = k_grad.astype(jnp.bfloat16).transpose(1, 0, 2).reshape(key_count, width)
    value_grad = v_grad.astype(jnp.bfloat16).transpose(1, 0, 2).reshape(key_count, width)
    return (going_back, gain_part, key_grad, value_grad)


def split_pieces(value, count):
    pieces = []
    rest = value
    for _ in range(count - 1):
        head = lax.reduce_precision(rest, exponent_bits=8, mantissa_bits=7)
        pieces.append(head)
        rest = rest - head
    pieces.append(rest)
    return jnp.stack(pieces).astype(jnp.bfloat16)


def shards(queries, out_grad, spec_keys, spec_values, owner_of, query_gain):
    peers = lax.axis_size("spec")
    cand_count = owner_of.shape[0]
    width = queries.shape[1]
    qtok_here = queries.shape[0] // cand_count
    slot_count = peers * CAP
    target = owner_of[:, 0]
    onehot = (target[:, None] == jnp.arange(peers, dtype=jnp.int32)[None, :]).astype(jnp.int32)
    earlier = jnp.cumsum(onehot, axis=0) - onehot
    position = jnp.sum(earlier * onehot, axis=1)
    slot_index = target * CAP + position
    matches = jnp.arange(slot_count, dtype=jnp.int32)[:, None] == slot_index[None, :]
    source = jnp.argmax(matches, axis=1).astype(jnp.int32)
    used = jnp.any(matches, axis=1)
    both = jnp.concatenate(
        [queries.reshape(cand_count, qtok_here, width), out_grad.reshape(cand_count, qtok_here, width)],
        axis=1,
    )
    source = jnp.where(used, source, cand_count)
    send_both = jnp.take(both, source, axis=0, mode="fill", fill_value=0)
    send_both = send_both.reshape(peers, CAP * 2 * qtok_here, width)
    recv_both = lax.all_to_all(send_both, "spec", split_axis=0, concat_axis=0, tiled=True)
    recv_both = recv_both.reshape(slot_count, 2, qtok_here, width)
    recv_rows = recv_both[:, 0].reshape(slot_count * qtok_here, width)
    recv_cotan = recv_both[:, 1].reshape(slot_count * qtok_here, width)
    going_back, partial_value, key_grad, value_grad = attend_backward(
        recv_rows, recv_cotan, spec_keys[0], spec_values[0], query_gain
    )
    going_back = going_back.reshape(peers, CAP * qtok_here, width)
    gain_rows = jnp.broadcast_to(split_pieces(partial_value, PIECES)[None], (peers, PIECES, width))
    going_back = jnp.concatenate([going_back, gain_rows], axis=1)
    came_back = lax.all_to_all(going_back, "spec", split_axis=0, concat_axis=0, tiled=True)
    spec_sum = jnp.sum(came_back[:, CAP * qtok_here :].astype(jnp.float32), axis=(0, 1))
    gain_grad = lax.psum(spec_sum, "grp")
    came_back = came_back[:, : CAP * qtok_here]
    home_grads = jnp.take(came_back.reshape(slot_count, qtok_here, width), slot_index, axis=0)
    query_grad = home_grads.reshape(cand_count * qtok_here, width)
    return (
        query_grad,
        key_grad[None],
        value_grad[None],
        gain_grad,
    )


def solution(mesh):
    return jax.shard_map(
        shards,
        mesh=mesh,
        in_specs=(
            P(("grp", "spec"), None),
            P(("grp", "spec"), None),
            P(("grp", "spec"), None, None),
            P(("grp", "spec"), None, None),
            P(("grp", "spec"), None),
            P(),
        ),
        out_specs=(
            P(("grp", "spec"), None),
            P(("grp", "spec"), None, None),
            P(("grp", "spec"), None, None),
            P(),
        ),
        check_vma=False,
    )
```

```python
import math

import jax
import jax.numpy as jnp
from jax import lax
from jax.sharding import PartitionSpec as P

HEADS = 8
HEAD_DIM = 128
CAP = 2
PIECES = 2


def attend_backward(recv_rows, recv_grads, keys_here, values_here, query_gain):
    total_rows, width = recv_rows.shape
    head_dim = width // HEADS
    key_count = keys_here.shape[0]
    inv_root = 1.0 / math.sqrt(HEAD_DIM)
    f32 = jnp.float32
    gain_hm = query_gain.reshape(HEADS, 1, head_dim)
    raw_hm = recv_rows.reshape(total_rows, HEADS, head_dim).transpose(1, 0, 2)
    g_hm = recv_grads.reshape(total_rows, HEADS, head_dim).transpose(1, 0, 2)
    k_hm = keys_here.reshape(key_count, HEADS, head_dim).transpose(1, 0, 2)
    v_hm = values_here.reshape(key_count, HEADS, head_dim).transpose(1, 0, 2)
    gained_hm = (raw_hm.astype(f32) * gain_hm).astype(jnp.bfloat16)
    scores = jnp.einsum("hrd,hkd->hrk", gained_hm, k_hm, preferred_element_type=f32) * inv_root
    top = jnp.max(scores, axis=2, keepdims=True)
    expo = jnp.exp(scores - top)
    probs = expo / jnp.sum(expo, axis=2, keepdims=True)
    probs_b = probs.astype(jnp.bfloat16)
    attended = jnp.einsum("hrk,hkd->hrd", probs_b, v_hm, preferred_element_type=f32)
    delta = jnp.sum(g_hm.astype(f32) * attended, axis=2, keepdims=True)
    dprobs = jnp.einsum("hrd,hkd->hrk", g_hm, v_hm, preferred_element_type=f32)
    dscores = (probs * (dprobs - delta)).astype(jnp.bfloat16)
    q_grad = jnp.einsum("hrk,hkd->hrd", dscores, k_hm, preferred_element_type=f32) * inv_root
    k_grad = jnp.einsum("hrk,hrd->hkd", dscores, gained_hm, preferred_element_type=f32) * inv_root
    v_grad = jnp.einsum("hrk,hrd->hkd", probs_b, g_hm, preferred_element_type=f32)
    gain_part = jnp.sum(raw_hm.astype(f32) * q_grad, axis=1).reshape(width)
    going_back = (q_grad * gain_hm).astype(jnp.bfloat16).transpose(1, 0, 2).reshape(total_rows, width)
    key_grad = k_grad.astype(jnp.bfloat16).transpose(1, 0, 2).reshape(key_count, width)
    value_grad = v_grad.astype(jnp.bfloat16).transpose(1, 0, 2).reshape(key_count, width)
    return (going_back, gain_part, key_grad, value_grad)


def split_pieces(value, count):
    pieces = []
    rest = value
    for _ in range(count - 1):
        head = lax.reduce_precision(rest, exponent_bits=8, mantissa_bits=7)
        pieces.append(head)
        rest = rest - head
    pieces.append(rest)
    return jnp.stack(pieces).astype(jnp.bfloat16)


def shards(queries, out_grad, spec_keys, spec_values, owner_of, query_gain):
    peers = lax.axis_size("spec")
    cand_count = owner_of.shape[0]
    width = queries.shape[1]
    qtok_here = queries.shape[0] // cand_count
    slot_count = peers * CAP
    target = owner_of[:, 0]
    onehot = (target[:, None] == jnp.arange(peers, dtype=jnp.int32)[None, :]).astype(jnp.int32)
    earlier = jnp.cumsum(onehot, axis=0) - onehot
    position = jnp.sum(earlier * onehot, axis=1)
    slot_index = target * CAP + position
    matches = jnp.arange(slot_count, dtype=jnp.int32)[:, None] == slot_index[None, :]
    source = jnp.argmax(matches, axis=1).astype(jnp.int32)
    used = jnp.any(matches, axis=1)
    both = jnp.concatenate(
        [queries.reshape(cand_count, qtok_here, width), out_grad.reshape(cand_count, qtok_here, width)],
        axis=1,
    )
    both = jnp.pad(both, ((0, 1), (0, 0), (0, 0)))
    source = jnp.where(used, source, cand_count)
    send_both = jnp.take(both, source, axis=0, mode="clip")
    send_both = send_both.reshape(peers, CAP * 2 * qtok_here, width)
    recv_both = lax.all_to_all(send_both, "spec", split_axis=0, concat_axis=0, tiled=True)
    recv_both = recv_both.reshape(slot_count, 2, qtok_here, width)
    recv_rows = recv_both[:, 0].reshape(slot_count * qtok_here, width)
    recv_cotan = recv_both[:, 1].reshape(slot_count * qtok_here, width)
    going_back, partial_value, key_grad, value_grad = attend_backward(
        recv_rows, recv_cotan, spec_keys[0], spec_values[0], query_gain
    )
    going_back = going_back.reshape(peers, CAP * qtok_here, width)
    gain_rows = jnp.broadcast_to(split_pieces(partial_value, PIECES)[None], (peers, PIECES, width))
    going_back = jnp.concatenate([going_back, gain_rows], axis=1)
    came_back = lax.all_to_all(going_back, "spec", split_axis=0, concat_axis=0, tiled=True)
    spec_sum = jnp.sum(came_back[:, CAP * qtok_here :].astype(jnp.float32), axis=(0, 1))
    gain_grad = lax.psum(spec_sum, "grp")
    came_back = came_back[:, : CAP * qtok_here]
    home_grads = jnp.take(
        came_back.reshape(slot_count, qtok_here, width), slot_index, axis=0, mode="clip"
    )
    query_grad = home_grads.reshape(cand_count * qtok_here, width)
    return (
        query_grad,
        key_grad[None],
        value_grad[None],
        gain_grad,
    )


def solution(mesh):
    return jax.shard_map(
        shards,
        mesh=mesh,
        in_specs=(
            P(("grp", "spec"), None),
            P(("grp", "spec"), None),
            P(("grp", "spec"), None, None),
            P(("grp", "spec"), None, None),
            P(("grp", "spec"), None),
            P(),
        ),
        out_specs=(
            P(("grp", "spec"), None),
            P(("grp", "spec"), None, None),
            P(("grp", "spec"), None, None),
            P(),
        ),
        check_vma=False,
    )
```

```python
import math

import jax
import jax.numpy as jnp
from jax import lax
from jax.sharding import PartitionSpec as P

HEADS = 8
HEAD_DIM = 128
CAP = 2
PIECES = 2


def attend_backward(recv_rows, recv_grads, keys_here, values_here, query_gain):
    total_rows, width = recv_rows.shape
    head_dim = width // HEADS
    key_count = keys_here.shape[0]
    inv_root = 1.0 / math.sqrt(HEAD_DIM)
    f32 = jnp.float32
    gain_hm = query_gain.reshape(HEADS, 1, head_dim)
    raw_hm = recv_rows.reshape(total_rows, HEADS, head_dim).transpose(1, 0, 2)
    g_hm = recv_grads.reshape(total_rows, HEADS, head_dim).transpose(1, 0, 2)
    k_hm = keys_here.reshape(key_count, HEADS, head_dim).transpose(1, 0, 2)
    v_hm = values_here.reshape(key_count, HEADS, head_dim).transpose(1, 0, 2)
    gained_hm = (raw_hm.astype(f32) * gain_hm).astype(jnp.bfloat16)
    scores = jnp.einsum("hrd,hkd->hrk", gained_hm, k_hm, preferred_element_type=f32) * inv_root
    top = jnp.max(scores, axis=2, keepdims=True)
    expo = jnp.exp(scores - top)
    probs = expo / jnp.sum(expo, axis=2, keepdims=True)
    probs_b = probs.astype(jnp.bfloat16)
    attended = jnp.einsum("hrk,hkd->hrd", probs_b, v_hm, preferred_element_type=f32)
    delta = jnp.sum(g_hm.astype(f32) * attended, axis=2, keepdims=True)
    dprobs = jnp.einsum("hrd,hkd->hrk", g_hm, v_hm, preferred_element_type=f32)
    dscores = (probs * (dprobs - delta)).astype(jnp.bfloat16)
    q_grad = jnp.einsum("hrk,hkd->hrd", dscores, k_hm, preferred_element_type=f32) * inv_root
    k_grad = jnp.einsum("hrk,hrd->hkd", dscores, gained_hm, preferred_element_type=f32) * inv_root
    v_grad = jnp.einsum("hrk,hrd->hkd", probs_b, g_hm, preferred_element_type=f32)
    gain_part = jnp.sum(raw_hm.astype(f32) * q_grad, axis=1).reshape(width)
    going_back = (q_grad * gain_hm).astype(jnp.bfloat16).transpose(1, 0, 2)
    key_grad = k_grad.astype(jnp.bfloat16).transpose(1, 0, 2).reshape(key_count, width)
    value_grad = v_grad.astype(jnp.bfloat16).transpose(1, 0, 2).reshape(key_count, width)
    return (going_back, gain_part, key_grad, value_grad)


def split_pieces(value, count):
    pieces = []
    rest = value
    for _ in range(count - 1):
        head = lax.reduce_precision(rest, exponent_bits=8, mantissa_bits=7)
        pieces.append(head)
        rest = rest - head
    pieces.append(rest)
    return jnp.stack(pieces).astype(jnp.bfloat16)


def shards(queries, out_grad, spec_keys, spec_values, owner_of, query_gain):
    peers = lax.axis_size("spec")
    cand_count = owner_of.shape[0]
    width = queries.shape[1]
    qtok_here = queries.shape[0] // cand_count
    slot_count = peers * CAP
    target = owner_of[:, 0]
    onehot = (target[:, None] == jnp.arange(peers, dtype=jnp.int32)[None, :]).astype(jnp.int32)
    earlier = jnp.cumsum(onehot, axis=0) - onehot
    position = jnp.sum(earlier * onehot, axis=1)
    slot_index = target * CAP + position
    matches = jnp.arange(slot_count, dtype=jnp.int32)[:, None] == slot_index[None, :]
    source = jnp.argmax(matches, axis=1).astype(jnp.int32)
    used = jnp.any(matches, axis=1)
    both = jnp.concatenate(
        [queries.reshape(cand_count, qtok_here, width), out_grad.reshape(cand_count, qtok_here, width)],
        axis=1,
    )
    both = jnp.pad(both, ((0, 1), (0, 0), (0, 0)))
    source = jnp.where(used, source, cand_count)
    send_both = jnp.take(both, source, axis=0, mode="clip")
    send_both = send_both.reshape(peers, CAP * 2 * qtok_here, width)
    recv_both = lax.all_to_all(send_both, "spec", split_axis=0, concat_axis=0, tiled=True)
    recv_both = recv_both.reshape(slot_count, 2, qtok_here, width)
    recv_rows = recv_both[:, 0].reshape(slot_count * qtok_here, width)
    recv_cotan = recv_both[:, 1].reshape(slot_count * qtok_here, width)
    going_back, partial_value, key_grad, value_grad = attend_backward(
        recv_rows, recv_cotan, spec_keys[0], spec_values[0], query_gain
    )
    going_back = going_back.reshape(peers, CAP * qtok_here, HEADS, width // HEADS)
    gain_rows = jnp.broadcast_to(
        split_pieces(partial_value, PIECES).reshape(1, PIECES, HEADS, width // HEADS),
        (peers, PIECES, HEADS, width // HEADS),
    )
    going_back = jnp.concatenate([going_back, gain_rows], axis=1)
    came_back = lax.all_to_all(going_back, "spec", split_axis=0, concat_axis=0, tiled=True)
    spec_sum = jnp.sum(came_back[:, CAP * qtok_here :].astype(jnp.float32), axis=(0, 1)).reshape(width)
    gain_grad = lax.psum(spec_sum, "grp")
    came_back = came_back[:, : CAP * qtok_here]
    home_grads = jnp.take(
        came_back.reshape(slot_count, qtok_here, HEADS, width // HEADS), slot_index, axis=0, mode="clip"
    )
    query_grad = home_grads.reshape(cand_count * qtok_here, width)
    return (
        query_grad,
        key_grad[None],
        value_grad[None],
        gain_grad,
    )


def solution(mesh):
    return jax.shard_map(
        shards,
        mesh=mesh,
        in_specs=(
            P(("grp", "spec"), None),
            P(("grp", "spec"), None),
            P(("grp", "spec"), None, None),
            P(("grp", "spec"), None, None),
            P(("grp", "spec"), None),
            P(),
        ),
        out_specs=(
            P(("grp", "spec"), None),
            P(("grp", "spec"), None, None),
            P(("grp", "spec"), None, None),
            P(),
        ),
        check_vma=False,
    )
```

```python
import math

import jax
import jax.numpy as jnp
from jax import lax
from jax.sharding import PartitionSpec as P

HEADS = 8
HEAD_DIM = 128
CAP = 2
PIECES = 2


def attend_backward(recv_rows, recv_grads, keys_here, values_here, query_gain):
    total_rows, _, head_dim = recv_rows.shape
    width = HEADS * head_dim
    key_count = keys_here.shape[0]
    inv_root = 1.0 / math.sqrt(HEAD_DIM)
    f32 = jnp.float32
    gain_hm = query_gain.reshape(HEADS, 1, head_dim)
    raw_hm = recv_rows.transpose(1, 0, 2)
    g_hm = recv_grads.transpose(1, 0, 2)
    k_hm = keys_here.reshape(key_count, HEADS, head_dim).transpose(1, 0, 2)
    v_hm = values_here.reshape(key_count, HEADS, head_dim).transpose(1, 0, 2)
    gained_hm = (raw_hm.astype(f32) * gain_hm).astype(jnp.bfloat16)
    scores = jnp.einsum("hrd,hkd->hrk", gained_hm, k_hm, preferred_element_type=f32) * inv_root
    top = jnp.max(scores, axis=2, keepdims=True)
    expo = jnp.exp(scores - top)
    probs = expo / jnp.sum(expo, axis=2, keepdims=True)
    probs_b = probs.astype(jnp.bfloat16)
    attended = jnp.einsum("hrk,hkd->hrd", probs_b, v_hm, preferred_element_type=f32)
    delta = jnp.sum(g_hm.astype(f32) * attended, axis=2, keepdims=True)
    dprobs = jnp.einsum("hrd,hkd->hrk", g_hm, v_hm, preferred_element_type=f32)
    dscores = (probs * (dprobs - delta)).astype(jnp.bfloat16)
    q_grad = jnp.einsum("hrk,hkd->hrd", dscores, k_hm, preferred_element_type=f32) * inv_root
    k_grad = jnp.einsum("hrk,hrd->hkd", dscores, gained_hm, preferred_element_type=f32) * inv_root
    v_grad = jnp.einsum("hrk,hrd->hkd", probs_b, g_hm, preferred_element_type=f32)
    gain_part = jnp.sum(raw_hm.astype(f32) * q_grad, axis=1).reshape(width)
    going_back = (q_grad * gain_hm).astype(jnp.bfloat16).transpose(1, 0, 2)
    key_grad = k_grad.astype(jnp.bfloat16).transpose(1, 0, 2).reshape(key_count, width)
    value_grad = v_grad.astype(jnp.bfloat16).transpose(1, 0, 2).reshape(key_count, width)
    return (going_back, gain_part, key_grad, value_grad)


def split_pieces(value, count):
    pieces = []
    rest = value
    for _ in range(count - 1):
        head = lax.reduce_precision(rest, exponent_bits=8, mantissa_bits=7)
        pieces.append(head)
        rest = rest - head
    pieces.append(rest)
    return jnp.stack(pieces).astype(jnp.bfloat16)


def shards(queries, out_grad, spec_keys, spec_values, owner_of, query_gain):
    peers = lax.axis_size("spec")
    cand_count = owner_of.shape[0]
    width = queries.shape[1]
    qtok_here = queries.shape[0] // cand_count
    slot_count = peers * CAP
    target = owner_of[:, 0]
    onehot = (target[:, None] == jnp.arange(peers, dtype=jnp.int32)[None, :]).astype(jnp.int32)
    earlier = jnp.cumsum(onehot, axis=0) - onehot
    position = jnp.sum(earlier * onehot, axis=1)
    slot_index = target * CAP + position
    matches = jnp.arange(slot_count, dtype=jnp.int32)[:, None] == slot_index[None, :]
    source = jnp.argmax(matches, axis=1).astype(jnp.int32)
    used = jnp.any(matches, axis=1)
    head_dim = width // HEADS
    both = jnp.concatenate(
        [
            queries.reshape(cand_count, qtok_here, HEADS, head_dim),
            out_grad.reshape(cand_count, qtok_here, HEADS, head_dim),
        ],
        axis=1,
    )
    both = jnp.pad(both, ((0, 1), (0, 0), (0, 0), (0, 0)))
    source = jnp.where(used, source, cand_count)
    send_both = jnp.take(both, source, axis=0, mode="clip")
    send_both = send_both.reshape(peers, CAP * 2 * qtok_here, HEADS, head_dim)
    recv_both = lax.all_to_all(send_both, "spec", split_axis=0, concat_axis=0, tiled=True)
    recv_both = recv_both.reshape(slot_count, 2, qtok_here, HEADS, head_dim)
    recv_rows = recv_both[:, 0].reshape(slot_count * qtok_here, HEADS, head_dim)
    recv_cotan = recv_both[:, 1].reshape(slot_count * qtok_here, HEADS, head_dim)
    going_back, partial_value, key_grad, value_grad = attend_backward(
        recv_rows, recv_cotan, spec_keys[0], spec_values[0], query_gain
    )
    going_back = going_back.reshape(peers, CAP * qtok_here, HEADS, width // HEADS)
    gain_rows = jnp.broadcast_to(
        split_pieces(partial_value, PIECES).reshape(1, PIECES, HEADS, width // HEADS),
        (peers, PIECES, HEADS, width // HEADS),
    )
    going_back = jnp.concatenate([going_back, gain_rows], axis=1)
    came_back = lax.all_to_all(going_back, "spec", split_axis=0, concat_axis=0, tiled=True)
    spec_sum = jnp.sum(came_back[:, CAP * qtok_here :].astype(jnp.float32), axis=(0, 1)).reshape(width)
    gain_grad = lax.psum(spec_sum, "grp")
    came_back = came_back[:, : CAP * qtok_here]
    home_grads = jnp.take(
        came_back.reshape(slot_count, qtok_here, HEADS, width // HEADS), slot_index, axis=0, mode="clip"
    )
    query_grad = home_grads.reshape(cand_count * qtok_here, width)
    return (
        query_grad,
        key_grad[None],
        value_grad[None],
        gain_grad,
    )


def solution(mesh):
    return jax.shard_map(
        shards,
        mesh=mesh,
        in_specs=(
            P(("grp", "spec"), None),
            P(("grp", "spec"), None),
            P(("grp", "spec"), None, None),
            P(("grp", "spec"), None, None),
            P(("grp", "spec"), None),
            P(),
        ),
        out_specs=(
            P(("grp", "spec"), None),
            P(("grp", "spec"), None, None),
            P(("grp", "spec"), None, None),
            P(),
        ),
        check_vma=False,
    )
```
